768 devices in a mesh: seq: 32 (over y, x), head: 24 (over z, core).
Axes of the slice: x: 4, y: 8, z: 12, core: 2. Of those that a mesh axis runs over, the one named last changes fastest.
Arguments:
- queries: bfloat16 [49152, 12288], P('seq', 'head'), may hold values from -70.26874 to 70.26874
- keys: bfloat16 [49152, 3072], P('seq', 'head'), may hold values from -6 to 6
- values: bfloat16 [49152, 3072], P('seq', 'head'), may hold values from -6 to 6
- file_lengths: int32 [3, 384], replicated, may hold values from 1 to 512, 49152 in all within a row
- owner_of: int32 [32, 32], P('seq'), may hold values from 0 to 31, each once within a row
Outputs:
- owned: bfloat16 [32, 32, 48, 12288], P('seq', None, 'head')
The draws below stay inside these ranges and needn't reach their ends.
Inputs may be any that keep to these rules, and one draw needn't show every extreme that they name: `owner_of`: row s names, for each of the 32 pieces of 48 tokens of shard s, its owner; each row names every owner once; the assignment is arbitrary.
All inputs are finite; a program needn't handle non-finite values.
Results may differ from the reference program's by a relative error of at most 0.0044.
Values may be sent and summed in bfloat16 or wider, within the bound.
No kernel may reach another device: no remote copies, remote signals or barrier semaphores. Data moves between devices by JAX's collectives and lax.ppermute only.
A program may use at most 32 MiB of HBM per device.

```python
import math
import jax
import jax.numpy as jnp
import numpy as np
from jax import lax

HD = 128
GROUP = 4
KV_HEADS = 8
FILE_MOST = 512
QROWS = 256
BATCH = 3
KV_ALL = 24
SHARDS = 32
TOKENS = 49152
PIECE = 48
FILES = 384


def paired_heads(key):
    base = jax.random.fold_in(key, 4711)
    key_query, key_key = jax.random.split(base)
    keys_out = jax.random.truncated_normal(key_key, -6.0, 6.0, (TOKENS, KV_ALL, HD), jnp.float32)
    queries_out = jax.random.truncated_normal(key_query, -6.0, 6.0, (TOKENS, KV_ALL, GROUP, HD), jnp.float32)
    return (queries_out.reshape(TOKENS, KV_ALL * GROUP * HD), keys_out.reshape(TOKENS, KV_ALL * HD))


def draw_queries(key, part):
    return paired_heads(key)[0].astype(jnp.bfloat16)


def draw_keys(key, part):
    return paired_heads(key)[1].astype(jnp.bfloat16)


def levels(rng, shape, cuts, low, top_value):
    def one(dim, blocks):
        heights = jax.random.uniform(jax.random.fold_in(jax.random.fold_in(rng, 6), dim), (blocks,), jnp.float32, low / len(cuts), top_value / len(cuts))
        return jnp.repeat(jnp.exp(heights), shape[dim] // blocks).reshape((-1,) + (1,) * (len(shape) - dim - 1))

    loudness = one(*cuts[0])
    for cut in cuts[1:]:
        loudness = loudness * one(*cut)
    return loudness


def profile(amount, total, reach, skew):
    weights = [(1 << 20) // math.isqrt(standing ** skew) + 1 for standing in range(2, amount + 1)]
    rest, given = total - reach - (amount - 1), [1] * (amount - 1)
    while rest > 0:
        candidates = [i for i in range(amount - 1) if given[i] < reach]
        pool, left = sum([weights[i] for i in candidates]), rest
        for i in candidates:
            more = min(reach - given[i], max(1, left * weights[i] // pool), rest)
            given[i] = given[i] + more
            rest = rest - more
    return np.array([reach] + given)


def uneven_parts(own_key, number_of, total, limit, skew):
    if number_of == 2:
        one = jax.random.randint(own_key, (), max(1, total - limit), min(limit, total - 1) + 1)
        return jnp.stack([one, total - one])
    tallies = jnp.asarray(profile(number_of, total, limit, skew), jnp.int32)
    couples = (number_of - 1) // 2
    donor, taker = tallies[1:1 + 2 * couples:2], tallies[2:2 + 2 * couples:2]
    slack = jnp.minimum(donor - 1, limit - taker)
    passed = jax.random.randint(jax.random.fold_in(own_key, 1), (couples,), 0, 1 << 20) % (slack + 1)
    tallies = tallies.at[1:1 + 2 * couples:2].set(donor - passed).at[2:2 + 2 * couples:2].set(taker + passed)
    return tallies[jax.random.permutation(jax.random.fold_in(own_key, 2), number_of)]


def bell_draw(own_key, extent, spread, limit, cuts=(), kind=jnp.bfloat16):
    array = jax.random.normal(own_key, extent, jnp.float32) * spread
    if len(cuts) > 0:
        array = levels(own_key, extent, cuts, -0.22, 0.18) * array
    return jnp.clip(array, min=-limit, max=limit).astype(kind)


def setup_inputs(seed: int = 0) -> dict:
    splits = jax.random.split(jax.random.key(seed), 6)
    queries = draw_queries(jax.random.fold_in(splits[5], 71), 0)
    keys = draw_keys(jax.random.fold_in(splits[5], 71), 0)
    values = bell_draw(splits[2], (TOKENS, KV_ALL * HD), 1.0, 6.0, ((0, 32), (1, 24)))
    file_lengths = jax.vmap(lambda own: uneven_parts(own, FILES, TOKENS, FILE_MOST, 2))(jax.random.split(splits[3], BATCH)).reshape((BATCH, FILES)).astype(jnp.int32)
    owner_of = jax.vmap(lambda own: jax.random.permutation(own, SHARDS))(jax.random.split(splits[4], SHARDS)).reshape((SHARDS, SHARDS)).astype(jnp.int32)
    return dict(queries=queries, keys=keys, values=values, file_lengths=file_lengths, owner_of=owner_of)


def doc_of(positions, file_ends):
    return jnp.searchsorted(file_ends, positions, side='right').astype(jnp.int32)

def attend_block(q_block, k_window, v_window, q_doc, k_doc, q_pos, k_pos, scale):
    scores = jnp.einsum('qgd,kd->gqk', q_block.astype(jnp.float32), k_window.astype(jnp.float32), precision=lax.Precision.HIGHEST) * scale
    allowed = (k_doc[None, :] == q_doc[:, None]) & (k_pos[None, :] <= q_pos[:, None]) & (k_pos[None, :] >= 0)
    scores = jnp.where(allowed[None, :, :], scores, -jnp.inf)
    row_max = lax.optimization_barrier(jnp.max(scores, axis=2, keepdims=True))
    expo = jnp.exp(scores - row_max)
    weights = (expo / lax.optimization_barrier(jnp.sum(expo, axis=2, keepdims=True))).astype(jnp.bfloat16)
    result = jnp.einsum('gqk,kd->qgd', weights.astype(jnp.float32), v_window.astype(jnp.float32), precision=lax.Precision.HIGHEST)
    return result.astype(jnp.bfloat16)

def reference(queries, keys, values, file_lengths, owner_of):
    file_ends = jnp.cumsum(file_lengths, axis=1).astype(jnp.int32)
    pad_keys = jnp.concatenate([jnp.zeros((FILE_MOST, KV_ALL * HD), keys.dtype), keys], axis=0)
    pad_values = jnp.concatenate([jnp.zeros((FILE_MOST, KV_ALL * HD), values.dtype), values], axis=0)
    positions = jnp.arange(TOKENS + FILE_MOST, dtype=jnp.int32) - FILE_MOST
    doc_table = jnp.stack([doc_of(positions, file_ends[index]) for index in range(BATCH)], axis=0)
    scale = 1.0 / math.sqrt(HD)

    def one_head(head_index):
        sequence = (head_index // KV_HEADS).astype(jnp.int32)
        doc_ids = lax.dynamic_index_in_dim(doc_table, sequence, 0, keepdims=False)
        q_head = lax.dynamic_slice_in_dim(queries, head_index * (GROUP * HD), GROUP * HD, 1).reshape(TOKENS, GROUP, HD)
        k_head = lax.dynamic_slice_in_dim(pad_keys, head_index * HD, HD, 1)
        v_head = lax.dynamic_slice_in_dim(pad_values, head_index * HD, HD, 1)

        def one_block(block_index):
            first = block_index * QROWS
            q_block = lax.dynamic_slice_in_dim(q_head, first, QROWS, 0)
            k_window = lax.dynamic_slice_in_dim(k_head, first, QROWS + FILE_MOST, 0)
            v_window = lax.dynamic_slice_in_dim(v_head, first, QROWS + FILE_MOST, 0)
            q_doc = lax.dynamic_slice_in_dim(doc_ids, first + FILE_MOST, QROWS, 0)
            k_doc = lax.dynamic_slice_in_dim(doc_ids, first, QROWS + FILE_MOST, 0)
            q_pos = lax.dynamic_slice_in_dim(positions, first + FILE_MOST, QROWS, 0)
            k_pos = lax.dynamic_slice_in_dim(positions, first, QROWS + FILE_MOST, 0)
            return attend_block(q_block, k_window, v_window, q_doc, k_doc, q_pos, k_pos, scale)
        blocks = lax.map(one_block, jnp.arange(TOKENS // QROWS, dtype=jnp.int32))
        return blocks.reshape(TOKENS, GROUP * HD)
    per_head = lax.map(one_head, jnp.arange(KV_ALL, dtype=jnp.int32))
    attended = jnp.transpose(per_head, (1, 0, 2)).reshape(TOKENS, KV_ALL * GROUP * HD)
    pieces = attended.reshape(SHARDS, SHARDS, PIECE, KV_ALL * GROUP * HD)
    inverse = jnp.argsort(owner_of, axis=1).astype(jnp.int32)
    by_owner = jnp.take_along_axis(pieces, inverse[:, :, None, None], axis=1)
    return jnp.transpose(by_owner, (1, 0, 2, 3))
```

```python
import math

import jax
import jax.numpy as jnp
from jax import lax
from jax.sharding import PartitionSpec as P

HD = 128
KV_HEADS = 8
FILE_MOST = 512
QROWS = 256


def from_behind(block, axis, distance):
    devices = range(lax.axis_size(axis))
    route = [(i - distance, i) for i in devices if i - distance in devices]
    return lax.ppermute(block, axis, route)


def attend_block(q_block, k_window, v_window, q_doc, k_doc, q_pos, k_pos, scale):
    scores = (
        jnp.einsum("qhgd,khd->hgqk", q_block, k_window, preferred_element_type=jnp.float32) * scale
    )
    allowed = (
        (k_doc[None, :] == q_doc[:, None])
        & (k_pos[None, :] <= q_pos[:, None])
        & (k_pos[None, :] >= 0)
    )
    scores = jnp.where(allowed[None, None, :, :], scores, -jnp.inf)
    row_max = jnp.max(scores, axis=3, keepdims=True)
    expo = jnp.exp(scores - row_max)
    weights = (expo / jnp.sum(expo, axis=3, keepdims=True)).astype(jnp.bfloat16)
    result = jnp.einsum("hgqk,khd->qhgd", weights, v_window, preferred_element_type=jnp.float32)
    return result.astype(jnp.bfloat16)


def stacked_windows(array, block_count, reach):
    tiles = array.reshape((block_count + reach, QROWS) + array.shape[1:])
    return jnp.concatenate([tiles[step : step + block_count] for step in range(reach + 1)], axis=1)


def per_device(queries, keys, values, file_lengths, owner_of):
    tok_rows = queries.shape[0]
    heads_here = keys.shape[1] // HD
    group_size = queries.shape[1] // keys.shape[1]
    shard_count = lax.axis_size("seq")
    offset = lax.axis_index("seq") * tok_rows
    sequence = lax.axis_index("head") * heads_here // KV_HEADS
    earlier = from_behind((keys, values), "seq", 1)
    rim_keys = earlier[0][tok_rows - FILE_MOST :]
    rim_values = earlier[1][tok_rows - FILE_MOST :]
    wide_keys = jnp.concatenate([rim_keys, keys], axis=0).reshape(
        tok_rows + FILE_MOST, heads_here, HD
    )
    wide_values = jnp.concatenate([rim_values, values], axis=0).reshape(
        tok_rows + FILE_MOST, heads_here, HD
    )
    file_count = file_lengths.shape[1]
    batch_pick = (jnp.arange(file_lengths.shape[0], dtype=jnp.int32) == sequence).astype(jnp.int32)
    lengths_here = jnp.sum(file_lengths * batch_pick[:, None], axis=0)
    file_index = jnp.arange(file_count, dtype=jnp.int32)
    upto = (file_index[:, None] <= file_index[None, :]).astype(jnp.int32)
    file_ends = jnp.sum(lengths_here[:, None] * upto, axis=0)
    positions = offset - FILE_MOST + jnp.arange(tok_rows + FILE_MOST, dtype=jnp.int32)
    doc_ids = jnp.sum((file_ends[None, :] <= positions[:, None]).astype(jnp.int32), axis=1)
    scale = 1.0 / math.sqrt(HD)
    block_count = tok_rows // QROWS
    reach = FILE_MOST // QROWS
    q_blocks = queries.reshape(block_count, QROWS, heads_here, group_size, HD)
    k_blocks = stacked_windows(wide_keys, block_count, reach)
    v_blocks = stacked_windows(wide_values, block_count, reach)
    kd_blocks = stacked_windows(doc_ids, block_count, reach)
    kp_blocks = stacked_windows(positions, block_count, reach)
    qd_blocks = doc_ids[FILE_MOST:].reshape(block_count, QROWS)
    qp_blocks = positions[FILE_MOST:].reshape(block_count, QROWS)

    def one_block(operands):
        q_block, k_window, v_window, q_doc, k_doc, q_pos, k_pos = operands
        return attend_block(q_block, k_window, v_window, q_doc, k_doc, q_pos, k_pos, scale)

    blocks = lax.map(
        one_block, (q_blocks, k_blocks, v_blocks, qd_blocks, kd_blocks, qp_blocks, kp_blocks)
    )
    attended = blocks.reshape(tok_rows, heads_here * group_size * HD)
    pieces = attended.reshape(shard_count, tok_rows // shard_count, heads_here * group_size * HD)
    owner_index = jnp.arange(shard_count, dtype=jnp.int32)
    one_hot = (owner_of[0][None, :] == owner_index[:, None]).astype(jnp.bfloat16)
    ordered = jnp.einsum("op,prc->orc", one_hot, pieces, preferred_element_type=jnp.float32).astype(
        jnp.bfloat16
    )
    head_count = lax.axis_size("head")
    rows_each = ordered.shape[1] // head_count
    chunks = ordered.reshape(shard_count * head_count, rows_each, ordered.shape[2])
    arrived = lax.all_to_all(chunks, ("seq", "head"), 0, 0, tiled=True)
    arrived = arrived.reshape(shard_count, head_count, rows_each, ordered.shape[2])
    arrived = jnp.transpose(arrived, (0, 2, 1, 3)).reshape(
        shard_count, rows_each, head_count * ordered.shape[2]
    )
    return arrived[None]


def solution(mesh):
    return jax.shard_map(
        per_device,
        mesh=mesh,
        in_specs=(P("seq", "head"), P("seq", "head"), P("seq", "head"), P(), P("seq", None)),
        out_specs=P("seq", None, "head", None),
        check_vma=False,
    )
```

```python
import functools
import math

import jax
import jax.numpy as jnp
from jax import lax
from jax.experimental import pallas as pl
from jax.sharding import PartitionSpec as P

HD = 128
KV_HEADS = 8
FILE_MOST = 512
QROWS = 256


def from_behind(block, axis, distance):
    devices = range(lax.axis_size(axis))
    route = [(i - distance, i) for i in devices if i - distance in devices]
    return lax.ppermute(block, axis, route)


def attend_kernel(q_ref, k_ref, v_ref, kd_ref, qd_ref, o_ref, *, scale, group):
    start = pl.multiple_of(pl.program_id(0) * QROWS, QROWS)
    k_window = k_ref[pl.ds(start, QROWS + FILE_MOST), :]
    v_window = v_ref[pl.ds(start, QROWS + FILE_MOST), :]
    row = lax.broadcasted_iota(jnp.int32, (QROWS, QROWS + FILE_MOST), 0)
    col = lax.broadcasted_iota(jnp.int32, (QROWS, QROWS + FILE_MOST), 1)
    allowed = (kd_ref[0] == qd_ref[...]) & (col <= row + FILE_MOST)
    for g in range(group):
        q_head = q_ref[:, g * HD : (g + 1) * HD]
        scores = (
            lax.dot_general(
                q_head, k_window, (((1,), (1,)), ((), ())), preferred_element_type=jnp.float32
            )
            * scale
        )
        scores = jnp.where(allowed, scores, -jnp.inf)
        row_max = jnp.max(scores, axis=1, keepdims=True)
        expo = jnp.exp(scores - row_max)
        weights = (expo / jnp.sum(expo, axis=1, keepdims=True)).astype(jnp.bfloat16)
        result = jnp.dot(weights, v_window, preferred_element_type=jnp.float32)
        o_ref[:, g * HD : (g + 1) * HD] = result.astype(o_ref.dtype)


def attend_local(queries, wide_keys, wide_values, kd_windows, q_doc, scale):
    tok_rows, width = queries.shape
    wide = wide_keys.shape[0]
    return pl.pallas_call(
        functools.partial(attend_kernel, scale=scale, group=width // HD),
        grid=(tok_rows // QROWS,),
        in_specs=[
            pl.BlockSpec((QROWS, width), lambda i: (i, 0)),
            pl.BlockSpec((wide, HD), lambda i: (0, 0)),
            pl.BlockSpec((wide, HD), lambda i: (0, 0)),
            pl.BlockSpec((1, 1, QROWS + FILE_MOST), lambda i: (i, 0, 0)),
            pl.BlockSpec((QROWS, 1), lambda i: (i, 0)),
        ],
        out_specs=pl.BlockSpec((QROWS, width), lambda i: (i, 0)),
        out_shape=jax.ShapeDtypeStruct((tok_rows, width), queries.dtype),
    )(queries, wide_keys, wide_values, kd_windows, q_doc)


def stacked_windows(array, block_count, reach):
    tiles = array.reshape((block_count + reach, QROWS) + array.shape[1:])
    return jnp.concatenate([tiles[step : step + block_count] for step in range(reach + 1)], axis=1)


def per_device(queries, keys, values, file_lengths, owner_of):
    tok_rows = queries.shape[0]
    heads_here = keys.shape[1] // HD
    shard_count = lax.axis_size("seq")
    head_count = lax.axis_size("head")
    offset = lax.axis_index("seq") * tok_rows
    sequence = lax.axis_index("head") * heads_here // KV_HEADS
    rim_keys, rim_values = from_behind(
        (keys[tok_rows - FILE_MOST :], values[tok_rows - FILE_MOST :]), "seq", 1
    )
    wide_keys = jnp.concatenate([rim_keys, keys], axis=0)
    wide_values = jnp.concatenate([rim_values, values], axis=0)
    file_count = file_lengths.shape[1]
    batch_pick = (jnp.arange(file_lengths.shape[0], dtype=jnp.int32) == sequence).astype(jnp.int32)
    lengths_here = jnp.sum(file_lengths * batch_pick[:, None], axis=0)
    file_index = jnp.arange(file_count, dtype=jnp.int32)
    upto = (file_index[:, None] <= file_index[None, :]).astype(jnp.int32)
    file_ends = jnp.sum(lengths_here[:, None] * upto, axis=0)
    positions = offset - FILE_MOST + jnp.arange(tok_rows + FILE_MOST, dtype=jnp.int32)
    doc_ids = jnp.sum((file_ends[None, :] <= positions[:, None]).astype(jnp.int32), axis=1)
    key_docs = jnp.where(positions >= 0, doc_ids, -1)
    scale = 1.0 / math.sqrt(HD)
    block_count = tok_rows // QROWS
    reach = FILE_MOST // QROWS
    kd_windows = stacked_windows(key_docs, block_count, reach).reshape(
        block_count, 1, QROWS + FILE_MOST
    )
    q_doc = doc_ids[FILE_MOST:].reshape(tok_rows, 1)
    if heads_here == 1:
        attended = attend_local(queries, wide_keys, wide_values, kd_windows, q_doc, scale)
    else:
        group_width = queries.shape[1] // heads_here
        attended = jnp.concatenate(
            [
                attend_local(
                    queries[:, h * group_width : (h + 1) * group_width],
                    wide_keys[:, h * HD : (h + 1) * HD],
                    wide_values[:, h * HD : (h + 1) * HD],
                    kd_windows,
                    q_doc,
                    scale,
                )
                for h in range(heads_here)
            ],
            axis=1,
        )
    pieces = attended.reshape(shard_count, tok_rows // shard_count, attended.shape[1])
    owner_index = jnp.arange(shard_count, dtype=jnp.int32)
    one_hot = (owner_of[0][None, :] == owner_index[:, None]).astype(jnp.bfloat16)
    ordered = jnp.einsum("op,prc->orc", one_hot, pieces, preferred_element_type=jnp.float32).astype(
        jnp.bfloat16
    )
    rows_each = ordered.shape[1] // head_count
    chunks = ordered.reshape(shard_count * head_count, rows_each, ordered.shape[2])
    arrived = lax.all_to_all(chunks, ("seq", "head"), 0, 0, tiled=True)
    arrived = arrived.reshape(shard_count, head_count, rows_each, ordered.shape[2])
    arrived = jnp.transpose(arrived, (0, 2, 1, 3)).reshape(
        shard_count, rows_each, head_count * ordered.shape[2]
    )
    return arrived[None]


def solution(mesh):
    return jax.shard_map(
        per_device,
        mesh=mesh,
        in_specs=(P("seq", "head"), P("seq", "head"), P("seq", "head"), P(), P("seq", None)),
        out_specs=P("seq", None, "head", None),
        check_vma=False,
    )
```

```python
import functools
import math

import jax
import jax.numpy as jnp
from jax import lax
from jax.experimental import pallas as pl
from jax.experimental.pallas import tpu as pltpu
from jax.sharding import PartitionSpec as P

HD = 128
KV_HEADS = 8
FILE_MOST = 512
QROWS = 256


def from_behind(block, axis, distance):
    devices = range(lax.axis_size(axis))
    route = [(i - distance, i) for i in devices if i - distance in devices]
    return lax.ppermute(block, axis, route)


def attend_kernel(owner_ref, offset_ref, q_ref, k_ref, v_ref, rk_ref, rv_ref, fe_row_ref, fe_col_ref,
                  o_ref, wide_k, wide_v, attended, *, scale, group, piece):
    step = pl.program_id(0)
    window = QROWS + FILE_MOST

    @pl.when(step == 0)
    def _():
        wide_k[0:FILE_MOST, :] = rk_ref[...]
        wide_k[FILE_MOST:, :] = k_ref[...]
        wide_v[0:FILE_MOST, :] = rv_ref[...]
        wide_v[FILE_MOST:, :] = v_ref[...]

    start = pl.multiple_of(step * QROWS, QROWS)
    k_window = wide_k[pl.ds(start, window), :]
    v_window = wide_v[pl.ds(start, window), :]
    first = offset_ref[0] + step * QROWS
    k_pos = first - FILE_MOST + lax.broadcasted_iota(jnp.int32, (1, window), 1)
    k_doc = jnp.sum((fe_col_ref[...] <= k_pos).astype(jnp.float32), axis=0, keepdims=True)
    k_doc = jnp.where(k_pos >= 0, k_doc, -1.0)
    q_pos = first + lax.broadcasted_iota(jnp.int32, (QROWS, 1), 0)
    q_doc = jnp.sum((fe_row_ref[...] <= q_pos).astype(jnp.float32), axis=1, keepdims=True)
    row = lax.broadcasted_iota(jnp.int32, (QROWS, window), 0)
    col = lax.broadcasted_iota(jnp.int32, (QROWS, window), 1)
    allowed = (k_doc == q_doc) & (col <= row + FILE_MOST)
    for g in range(group):
        q_head = q_ref[:, g * HD:(g + 1) * HD]
        scores = lax.dot_general(q_head, k_window, (((1,), (1,)), ((), ())),
                                 preferred_element_type=jnp.float32) * scale
        scores = jnp.where(allowed, scores, -jnp.inf)
        row_max = jnp.max(scores, axis=1, keepdims=True)
        expo = jnp.exp(scores - row_max)
        weights = (expo / jnp.sum(expo, axis=1, keepdims=True)).astype(jnp.bfloat16)
        result = jnp.dot(weights, v_window, preferred_element_type=jnp.float32)
        attended[pl.ds(start, QROWS), g * HD:(g + 1) * HD] = result.astype(attended.dtype)

    @pl.when(step == pl.num_programs(0) - 1)
    def _():
        for p in range(o_ref.shape[0]):
            o_ref[owner_ref[p]] = attended[p * piece:(p + 1) * piece, :]

def attend_ordered(owner_row, offset, queries, keys, values, rim_keys, rim_values, file_ends, scale):
    tok_rows, width = queries.shape
    shard_count = owner_row.shape[0]
    piece = tok_rows // shard_count
    fe_row = file_ends.reshape(1, -1)
    fe_col = file_ends.reshape(-1, 1)
    full = lambda shape: pl.BlockSpec(shape, lambda i, *_: (0,) * len(shape))
    grid_spec = pltpu.PrefetchScalarGridSpec(
        num_scalar_prefetch=2,
        grid=(tok_rows // QROWS,),
        in_specs=[
            pl.BlockSpec((QROWS, width), lambda i, *_: (i, 0)),
            full(keys.shape), full(values.shape), full(rim_keys.shape), full(rim_values.shape),
            full(fe_row.shape), full(fe_col.shape),
        ],
        out_specs=full((shard_count, piece, width)),
        scratch_shapes=[
            pltpu.VMEM((tok_rows + FILE_MOST, HD), keys.dtype),
            pltpu.VMEM((tok_rows + FILE_MOST, HD), values.dtype),
            pltpu.VMEM((tok_rows, width), queries.dtype),
        ],
    )
    return pl.pallas_call(
        functools.partial(attend_kernel, scale=scale, group=width // HD, piece=piece),
        grid_spec=grid_spec,
        out_shape=jax.ShapeDtypeStruct((shard_count, piece, width), queries.dtype),
        compiler_params=pltpu.CompilerParams(dimension_semantics=("arbitrary",)),
    )(owner_row, offset, queries, keys, values, rim_keys, rim_values, fe_row, fe_col)


def per_device(queries, keys, values, file_lengths, owner_of):
    tok_rows = queries.shape[0]
    heads_here = keys.shape[1] // HD
    shard_count = lax.axis_size("seq")
    head_count = lax.axis_size("head")
    offset = lax.axis_index("seq") * tok_rows
    sequence = lax.axis_index("head") * heads_here // KV_HEADS
    rim_keys, rim_values = from_behind(
        (keys[tok_rows - FILE_MOST :], values[tok_rows - FILE_MOST :]), "seq", 1
    )
    file_count = file_lengths.shape[1]
    batch_pick = (jnp.arange(file_lengths.shape[0], dtype=jnp.int32) == sequence).astype(jnp.int32)
    lengths_here = jnp.sum(file_lengths * batch_pick[:, None], axis=0)
    file_index = jnp.arange(file_count, dtype=jnp.int32)
    upto = (file_index[:, None] <= file_index[None, :]).astype(jnp.int32)
    file_ends = jnp.sum(lengths_here[:, None] * upto, axis=0)
    scale = 1.0 / math.sqrt(HD)
    ordered = attend_ordered(
        owner_of[0].astype(jnp.int32),
        jnp.reshape(offset, (1,)).astype(jnp.int32),
        queries,
        keys,
        values,
        rim_keys,
        rim_values,
        file_ends,
        scale,
    )
    rows_each = ordered.shape[1] // head_count
    chunks = ordered.reshape(shard_count * head_count, rows_each, ordered.shape[2])
    arrived = lax.all_to_all(chunks, ("seq", "head"), 0, 0, tiled=True)
    arrived = arrived.reshape(shard_count, head_count, rows_each, ordered.shape[2])
    arrived = jnp.transpose(arrived, (0, 2, 1, 3)).reshape(
        shard_count, rows_each, head_count * ordered.shape[2]
    )
    return arrived[None]


def solution(mesh):
    return jax.shard_map(
        per_device,
        mesh=mesh,
        in_specs=(P("seq", "head"), P("seq", "head"), P("seq", "head"), P(), P("seq", None)),
        out_specs=P("seq", None, "head", None),
        check_vma=False,
    )
```

```python
import functools
import math

import jax
import jax.numpy as jnp
from jax import lax
from jax.experimental import pallas as pl
from jax.experimental.pallas import tpu as pltpu
from jax.sharding import PartitionSpec as P

HD = 128
KV_HEADS = 8
FILE_MOST = 512
QROWS = 256
TRIM = 128
TRIMS = 2


def from_behind(block, axis, distance):
    devices = range(lax.axis_size(axis))
    route = [(i - distance, i) for i in devices if i - distance in devices]
    return lax.ppermute(block, axis, route)


def attend_kernel(owner_ref, offset_ref, trim_ref, q_ref, k_ref, v_ref, rim_ref, fe_row_ref, fe_col_ref,
                  o_ref, wide_k, wide_v, attended, *, scale, group, piece):
    step = pl.program_id(0)

    @pl.when(step == 0)
    def _():
        wide_k[0:FILE_MOST, :] = rim_ref[:, 0:HD]
        wide_k[FILE_MOST:, :] = k_ref[...]
        wide_v[0:FILE_MOST, :] = rim_ref[:, HD:2 * HD]
        wide_v[FILE_MOST:, :] = v_ref[...]

    start = pl.multiple_of(step * QROWS, QROWS)
    first = offset_ref[0] + step * QROWS
    q_pos = first + lax.broadcasted_iota(jnp.int32, (QROWS, 1), 0)
    q_doc = jnp.sum((fe_row_ref[...] <= q_pos).astype(jnp.float32), axis=1, keepdims=True)

    def attend(lo):
        window = QROWS + FILE_MOST - lo
        k_window = wide_k[pl.ds(pl.multiple_of(start + lo, TRIM), window), :]
        v_window = wide_v[pl.ds(pl.multiple_of(start + lo, TRIM), window), :]
        k_pos = first - FILE_MOST + lo + lax.broadcasted_iota(jnp.int32, (1, window), 1)
        k_doc = jnp.sum((fe_col_ref[...] <= k_pos).astype(jnp.float32), axis=0, keepdims=True)
        k_doc = jnp.where(k_pos >= 0, k_doc, -1.0)
        row = lax.broadcasted_iota(jnp.int32, (QROWS, window), 0)
        col = lax.broadcasted_iota(jnp.int32, (QROWS, window), 1)
        allowed = (k_doc == q_doc) & (col + lo <= row + FILE_MOST)
        for g in range(group):
            q_head = q_ref[:, g * HD:(g + 1) * HD]
            scores = lax.dot_general(q_head, k_window, (((1,), (1,)), ((), ())),
                                     preferred_element_type=jnp.float32) * scale
            scores = jnp.where(allowed, scores, -jnp.inf)
            row_max = jnp.max(scores, axis=1, keepdims=True)
            expo = jnp.exp(scores - row_max)
            weights = (expo / jnp.sum(expo, axis=1, keepdims=True)).astype(jnp.bfloat16)
            result = jnp.dot(weights, v_window, preferred_element_type=jnp.float32)
            attended[pl.ds(start, QROWS), g * HD:(g + 1) * HD] = result.astype(attended.dtype)

    for t in range(TRIMS + 1):
        pl.when(trim_ref[step] == t)(functools.partial(attend, t * TRIM))

    @pl.when(step == pl.num_programs(0) - 1)
    def _():
        for p in range(o_ref.shape[0]):
            o_ref[owner_ref[p]] = attended[p * piece:(p + 1) * piece, :]

def leading_trims(offset, file_ends, block_count):
    firsts = offset + QROWS * jnp.arange(block_count, dtype=jnp.int32)
    starts = jnp.max(jnp.where(file_ends[None, :] <= firsts[:, None], file_ends[None, :], 0), axis=1)
    lasts = firsts[:, None] - FILE_MOST + TRIM - 1 + TRIM * jnp.arange(TRIMS, dtype=jnp.int32)[None, :]
    return jnp.sum((lasts < starts[:, None]).astype(jnp.int32), axis=1)

def attend_ordered(owner_row, offset, queries, keys, values, rim, file_ends, scale):
    tok_rows, width = queries.shape
    shard_count = owner_row.shape[0]
    piece = tok_rows // shard_count
    block_count = tok_rows // QROWS
    trims = leading_trims(offset, file_ends, block_count)
    fe_row = file_ends.reshape(1, -1)
    fe_col = file_ends.reshape(-1, 1)
    full = lambda shape: pl.BlockSpec(shape, lambda i, *_: (0,) * len(shape))
    grid_spec = pltpu.PrefetchScalarGridSpec(
        num_scalar_prefetch=3,
        grid=(block_count,),
        in_specs=[
            pl.BlockSpec((QROWS, width), lambda i, *_: (i, 0)),
            full(keys.shape), full(values.shape), full(rim.shape),
            full(fe_row.shape), full(fe_col.shape),
        ],
        out_specs=full((shard_count, piece, width)),
        scratch_shapes=[
            pltpu.VMEM((tok_rows + FILE_MOST, HD), keys.dtype),
            pltpu.VMEM((tok_rows + FILE_MOST, HD), values.dtype),
            pltpu.VMEM((tok_rows, width), queries.dtype),
        ],
    )
    return pl.pallas_call(
        functools.partial(attend_kernel, scale=scale, group=width // HD, piece=piece),
        grid_spec=grid_spec,
        out_shape=jax.ShapeDtypeStruct((shard_count, piece, width), queries.dtype),
        compiler_params=pltpu.CompilerParams(dimension_semantics=("arbitrary",)),
    )(owner_row, jnp.reshape(offset, (1,)), trims, queries, keys, values, rim, fe_row, fe_col)


def per_device(queries, keys, values, file_lengths, owner_of):
    tok_rows = queries.shape[0]
    heads_here = keys.shape[1] // HD
    shard_count = lax.axis_size("seq")
    head_count = lax.axis_size("head")
    offset = lax.axis_index("seq") * tok_rows
    sequence = lax.axis_index("head") * heads_here // KV_HEADS
    rim = from_behind(
        jnp.concatenate([keys[tok_rows - FILE_MOST :], values[tok_rows - FILE_MOST :]], axis=1),
        "seq",
        1,
    )
    file_count = file_lengths.shape[1]
    batch_pick = (jnp.arange(file_lengths.shape[0], dtype=jnp.int32) == sequence).astype(jnp.int32)
    lengths_here = jnp.sum(file_lengths * batch_pick[:, None], axis=0)
    file_index = jnp.arange(file_count, dtype=jnp.int32)
    upto = (file_index[:, None] <= file_index[None, :]).astype(jnp.int32)
    file_ends = jnp.sum(lengths_here[:, None] * upto, axis=0)
    scale = 1.0 / math.sqrt(HD)
    ordered = attend_ordered(
        owner_of[0].astype(jnp.int32),
        offset.astype(jnp.int32),
        queries,
        keys,
        values,
        rim,
        file_ends,
        scale,
    )
    rows_each = ordered.shape[1] // head_count
    chunks = ordered.reshape(shard_count * head_count, rows_each, ordered.shape[2])
    arrived = lax.all_to_all(chunks, ("seq", "head"), 0, 0, tiled=True)
    arrived = arrived.reshape(shard_count, head_count, rows_each, ordered.shape[2])
    arrived = jnp.transpose(arrived, (0, 2, 1, 3)).reshape(
        shard_count, rows_each, head_count * ordered.shape[2]
    )
    return arrived[None]


def solution(mesh):
    return jax.shard_map(
        per_device,
        mesh=mesh,
        in_specs=(P("seq", "head"), P("seq", "head"), P("seq", "head"), P(), P("seq", None)),
        out_specs=P("seq", None, "head", None),
        check_vma=False,
    )
```

```python
import functools
import math

import jax
import jax.numpy as jnp
from jax import lax
from jax.experimental import pallas as pl
from jax.experimental.pallas import tpu as pltpu
from jax.sharding import PartitionSpec as P

HD = 128
KV_HEADS = 8
FILE_MOST = 512
QROWS = 256
TRIM = 128
TRIMS = 2


def from_behind(block, axis, distance):
    devices = range(lax.axis_size(axis))
    route = [(i - distance, i) for i in devices if i - distance in devices]
    return lax.ppermute(block, axis, route)


def attend_kernel(owner_ref, offset_ref, trim_ref, q_ref, k_ref, v_ref, rim_ref, fe_row_ref, fe_col_ref,
                  o_ref, wide_k, wide_v, attended, *, scale, group, piece):
    step = pl.program_id(0)

    @pl.when(step == 0)
    def _():
        wide_k[0:FILE_MOST, :] = rim_ref[:, 0:HD]
        wide_k[FILE_MOST:, :] = k_ref[...]
        wide_v[0:FILE_MOST, :] = rim_ref[:, HD:2 * HD]
        wide_v[FILE_MOST:, :] = v_ref[...]

    start = pl.multiple_of(step * QROWS, QROWS)
    first = offset_ref[0] + step * QROWS
    q_pos = first + lax.broadcasted_iota(jnp.int32, (QROWS, 1), 0)
    q_doc = jnp.sum((fe_row_ref[...] <= q_pos).astype(jnp.float32), axis=1, keepdims=True)

    def attend(lo):
        window = QROWS + FILE_MOST - lo
        k_window = wide_k[pl.ds(pl.multiple_of(start + lo, TRIM), window), :]
        v_window = wide_v[pl.ds(pl.multiple_of(start + lo, TRIM), window), :]
        k_pos = first - FILE_MOST + lo + lax.broadcasted_iota(jnp.int32, (1, window), 1)
        k_doc = jnp.sum((fe_col_ref[...] <= k_pos).astype(jnp.float32), axis=0, keepdims=True)
        k_doc = jnp.where(k_pos >= 0, k_doc, -1.0)
        row = lax.broadcasted_iota(jnp.int32, (QROWS, window), 0)
        col = lax.broadcasted_iota(jnp.int32, (QROWS, window), 1)
        allowed = (k_doc == q_doc) & (col + lo <= row + FILE_MOST)
        for g in range(group):
            q_head = q_ref[:, g * HD:(g + 1) * HD]
            scores = lax.dot_general(q_head, k_window, (((1,), (1,)), ((), ())),
                                     preferred_element_type=jnp.float32) * scale
            scores = jnp.where(allowed, scores, -jnp.inf)
            row_max = jnp.max(scores, axis=1, keepdims=True)
            expo = jnp.exp(scores - row_max)
            weights = (expo / jnp.sum(expo, axis=1, keepdims=True)).astype(jnp.bfloat16)
            result = jnp.dot(weights, v_window, preferred_element_type=jnp.float32)
            attended[pl.ds(start, QROWS), g * HD:(g + 1) * HD] = result.astype(attended.dtype)

    for t in range(TRIMS + 1):
        pl.when(trim_ref[step] == t)(functools.partial(attend, t * TRIM))

    @pl.when(step == pl.num_programs(0) - 1)
    def _():
        for p in range(o_ref.shape[0]):
            o_ref[owner_ref[p]] = attended[p * piece:(p + 1) * piece, :]

def leading_trims(offset, file_ends, block_count):
    firsts = offset + QROWS * jnp.arange(block_count, dtype=jnp.int32)
    starts = jnp.max(jnp.where(file_ends[None, :] <= firsts[:, None], file_ends[None, :], 0), axis=1)
    lasts = firsts[:, None] - FILE_MOST + TRIM - 1 + TRIM * jnp.arange(TRIMS, dtype=jnp.int32)[None, :]
    return jnp.sum((lasts < starts[:, None]).astype(jnp.int32), axis=1)

def attend_ordered(owner_row, offset, queries, keys, values, rim, file_ends, scale):
    tok_rows, width = queries.shape
    shard_count = owner_row.shape[0]
    piece = tok_rows // shard_count
    block_count = tok_rows // QROWS
    trims = leading_trims(offset, file_ends, block_count)
    fe_row = file_ends.reshape(1, -1)
    fe_col = file_ends.reshape(-1, 1)
    full = lambda shape: pl.BlockSpec(shape, lambda i, *_: (0,) * len(shape))
    grid_spec = pltpu.PrefetchScalarGridSpec(
        num_scalar_prefetch=3,
        grid=(block_count,),
        in_specs=[
            pl.BlockSpec((QROWS, width), lambda i, *_: (i, 0)),
            full(keys.shape), full(values.shape), full(rim.shape),
            full(fe_row.shape), full(fe_col.shape),
        ],
        out_specs=full((shard_count, piece, width)),
        scratch_shapes=[
            pltpu.VMEM((tok_rows + FILE_MOST, HD), keys.dtype),
            pltpu.VMEM((tok_rows + FILE_MOST, HD), values.dtype),
            pltpu.VMEM((tok_rows, width), queries.dtype),
        ],
    )
    return pl.pallas_call(
        functools.partial(attend_kernel, scale=scale, group=width // HD, piece=piece),
        grid_spec=grid_spec,
        out_shape=jax.ShapeDtypeStruct((shard_count, piece, width), queries.dtype),
        compiler_params=pltpu.CompilerParams(dimension_semantics=("arbitrary",)),
    )(owner_row, jnp.reshape(offset, (1,)), trims, queries, keys, values, rim, fe_row, fe_col)


def place_kernel(src_ref, dst_ref, sems):
    heads = src_ref.shape[1]
    width = src_ref.shape[3]
    copies = [
        pltpu.make_async_copy(
            src_ref.at[:, h], dst_ref.at[:, :, pl.ds(h * width, width)], sems.at[h]
        )
        for h in range(heads)
    ]
    for copy in copies:
        copy.start()
    for copy in copies:
        copy.wait()


def place_rows(arrived):
    shard_count, heads, rows, width = arrived.shape
    return pl.pallas_call(
        place_kernel,
        in_specs=[pl.BlockSpec(memory_space=pl.ANY)],
        out_specs=pl.BlockSpec(memory_space=pl.ANY),
        out_shape=jax.ShapeDtypeStruct((shard_count, rows, heads * width), arrived.dtype),
        scratch_shapes=[pltpu.SemaphoreType.DMA((heads,))],
    )(arrived)


def per_device(queries, keys, values, file_lengths, owner_of):
    tok_rows = queries.shape[0]
    heads_here = keys.shape[1] // HD
    shard_count = lax.axis_size("seq")
    head_count = lax.axis_size("head")
    offset = lax.axis_index("seq") * tok_rows
    sequence = lax.axis_index("head") * heads_here // KV_HEADS
    rim = from_behind(
        jnp.concatenate([keys[tok_rows - FILE_MOST :], values[tok_rows - FILE_MOST :]], axis=1),
        "seq",
        1,
    )
    file_count = file_lengths.shape[1]
    batch_pick = (jnp.arange(file_lengths.shape[0], dtype=jnp.int32) == sequence).astype(jnp.int32)
    lengths_here = jnp.sum(file_lengths * batch_pick[:, None], axis=0)
    file_index = jnp.arange(file_count, dtype=jnp.int32)
    upto = (file_index[:, None] <= file_index[None, :]).astype(jnp.int32)
    file_ends = jnp.sum(lengths_here[:, None] * upto, axis=0)
    scale = 1.0 / math.sqrt(HD)
    ordered = attend_ordered(
        owner_of[0].astype(jnp.int32),
        offset.astype(jnp.int32),
        queries,
        keys,
        values,
        rim,
        file_ends,
        scale,
    )
    rows_each = ordered.shape[1] // head_count
    chunks = ordered.reshape(shard_count * head_count, rows_each, ordered.shape[2])
    arrived = lax.all_to_all(chunks, ("seq", "head"), 0, 0, tiled=True)
    arrived = arrived.reshape(shard_count, head_count, rows_each, ordered.shape[2])
    return place_rows(arrived)[None]


def solution(mesh):
    return jax.shard_map(
        per_device,
        mesh=mesh,
        in_specs=(P("seq", "head"), P("seq", "head"), P("seq", "head"), P(), P("seq", None)),
        out_specs=P("seq", None, "head", None),
        check_vma=False,
    )
```

```python
import functools
import math

import jax
import jax.numpy as jnp
from jax import lax
from jax.experimental import pallas as pl
from jax.experimental.pallas import tpu as pltpu
from jax.sharding import PartitionSpec as P

HD = 128
KV_HEADS = 8
FILE_MOST = 512
QROWS = 256
TRIM = 128
TRIMS = 2


def from_behind(block, axis, distance):
    devices = range(lax.axis_size(axis))
    route = [(i - distance, i) for i in devices if i - distance in devices]
    return lax.ppermute(block, axis, route)


def attend_rows(q_ref, k_src, fe_row_ref, fe_col_ref, out_ref, out_start, k_start, first, lo, scale):
    window = QROWS + FILE_MOST - lo
    k_window = k_src[0][pl.ds(pl.multiple_of(k_start + lo, TRIM), window), :]
    v_window = k_src[1][pl.ds(pl.multiple_of(k_start + lo, TRIM), window), :]
    q_pos = first + lax.broadcasted_iota(jnp.int32, (QROWS, 1), 0)
    q_doc = jnp.sum((fe_row_ref[...] <= q_pos).astype(jnp.float32), axis=1, keepdims=True)
    k_pos = first - FILE_MOST + lo + lax.broadcasted_iota(jnp.int32, (1, window), 1)
    k_doc = jnp.sum((fe_col_ref[...] <= k_pos).astype(jnp.float32), axis=0, keepdims=True)
    k_doc = jnp.where(k_pos >= 0, k_doc, -1.0)
    row = lax.broadcasted_iota(jnp.int32, (QROWS, window), 0)
    col = lax.broadcasted_iota(jnp.int32, (QROWS, window), 1)
    allowed = (k_doc == q_doc) & (col + lo <= row + FILE_MOST)
    for g in range(q_ref.shape[1] // HD):
        q_head = q_ref[:, g * HD : (g + 1) * HD]
        scores = (
            lax.dot_general(
                q_head, k_window, (((1,), (1,)), ((), ())), preferred_element_type=jnp.float32
            )
            * scale
        )
        scores = jnp.where(allowed, scores, -jnp.inf)
        row_max = jnp.max(scores, axis=1, keepdims=True)
        expo = jnp.exp(scores - row_max)
        weights = (expo / jnp.sum(expo, axis=1, keepdims=True)).astype(jnp.bfloat16)
        result = jnp.dot(weights, v_window, preferred_element_type=jnp.float32)
        out_ref[pl.ds(out_start, QROWS), g * HD : (g + 1) * HD] = result.astype(out_ref.dtype)


def later_kernel(offset_ref, trim_ref, q_ref, k_ref, v_ref, fe_row_ref, fe_col_ref, o_ref, *, scale, skip):
    step = pl.program_id(0)
    block = step + skip
    k_start = pl.multiple_of(block * QROWS - FILE_MOST, QROWS)
    first = offset_ref[0] + block * QROWS
    for t in range(TRIMS + 1):
        pl.when(trim_ref[block] == t)(
            functools.partial(
                attend_rows, q_ref, (k_ref, v_ref), fe_row_ref, fe_col_ref, o_ref, 0, k_start, first,
                t * TRIM, scale,
            )
        )


def early_kernel(owner_ref, offset_ref, trim_ref, q_ref, k_ref, v_ref, rim_ref, fe_row_ref, fe_col_ref,
                 later_ref, o_ref, wide_k, wide_v, attended, *, scale, piece):
    step = pl.program_id(0)
    lead = wide_k.shape[0] - FILE_MOST

    @pl.when(step == 0)
    def _():
        wide_k[0:FILE_MOST, :] = rim_ref[:, 0:HD]
        wide_k[FILE_MOST:, :] = k_ref[0:lead, :]
        wide_v[0:FILE_MOST, :] = rim_ref[:, HD : 2 * HD]
        wide_v[FILE_MOST:, :] = v_ref[0:lead, :]
        attended[lead:, :] = later_ref[lead:, :]

    start = pl.multiple_of(step * QROWS, QROWS)
    first = offset_ref[0] + step * QROWS
    for t in range(TRIMS + 1):
        pl.when(trim_ref[step] == t)(
            functools.partial(
                attend_rows, q_ref, (wide_k, wide_v), fe_row_ref, fe_col_ref, attended, start, start,
                first, t * TRIM, scale,
            )
        )

    @pl.when(step == pl.num_programs(0) - 1)
    def _():
        for p in range(o_ref.shape[0]):
            o_ref[owner_ref[p]] = attended[p * piece : (p + 1) * piece, :]


def leading_trims(offset, file_ends, block_count):
    firsts = offset + QROWS * jnp.arange(block_count, dtype=jnp.int32)
    starts = jnp.max(jnp.where(file_ends[None, :] <= firsts[:, None], file_ends[None, :], 0), axis=1)
    lasts = firsts[:, None] - FILE_MOST + TRIM - 1 + TRIM * jnp.arange(TRIMS, dtype=jnp.int32)[None, :]
    return jnp.sum((lasts < starts[:, None]).astype(jnp.int32), axis=1)

def attend_ordered(owner_row, offset, queries, keys, values, rim, file_ends, scale):
    tok_rows, width = queries.shape
    shard_count = owner_row.shape[0]
    piece = tok_rows // shard_count
    block_count = tok_rows // QROWS
    early = FILE_MOST // QROWS
    trims = leading_trims(offset, file_ends, block_count)
    offset_row = jnp.reshape(offset, (1,))
    fe_row = file_ends.reshape(1, -1)
    fe_col = file_ends.reshape(-1, 1)
    full = lambda shape: pl.BlockSpec(shape, lambda i, *_: (0,) * len(shape))
    params = pltpu.CompilerParams(dimension_semantics=("arbitrary",))
    later = pl.pallas_call(
        functools.partial(later_kernel, scale=scale, skip=early),
        grid_spec=pltpu.PrefetchScalarGridSpec(
            num_scalar_prefetch=2,
            grid=(block_count - early,),
            in_specs=[
                pl.BlockSpec((QROWS, width), lambda i, *_: (i + early, 0)),
                full(keys.shape), full(values.shape), full(fe_row.shape), full(fe_col.shape),
            ],
            out_specs=pl.BlockSpec((QROWS, width), lambda i, *_: (i + early, 0)),
        ),
        out_shape=jax.ShapeDtypeStruct((tok_rows, width), queries.dtype),
        compiler_params=params,
    )(offset_row, trims, queries, keys, values, fe_row, fe_col)
    return pl.pallas_call(
        functools.partial(early_kernel, scale=scale, piece=piece),
        grid_spec=pltpu.PrefetchScalarGridSpec(
            num_scalar_prefetch=3,
            grid=(early,),
            in_specs=[
                pl.BlockSpec((QROWS, width), lambda i, *_: (i, 0)),
                full(keys.shape), full(values.shape), full(rim.shape),
                full(fe_row.shape), full(fe_col.shape), full(later.shape),
            ],
            out_specs=full((shard_count, piece, width)),
            scratch_shapes=[
                pltpu.VMEM((2 * FILE_MOST, HD), keys.dtype),
                pltpu.VMEM((2 * FILE_MOST, HD), values.dtype),
                pltpu.VMEM((tok_rows, width), queries.dtype),
            ],
        ),
        out_shape=jax.ShapeDtypeStruct((shard_count, piece, width), queries.dtype),
        compiler_params=params,
    )(owner_row, offset_row, trims, queries, keys, values, rim, fe_row, fe_col, later)


def per_device(queries, keys, values, file_lengths, owner_of):
    tok_rows = queries.shape[0]
    heads_here = keys.shape[1] // HD
    shard_count = lax.axis_size("seq")
    head_count = lax.axis_size("head")
    offset = lax.axis_index("seq") * tok_rows
    sequence = lax.axis_index("head") * heads_here // KV_HEADS
    rim = from_behind(
        jnp.concatenate([keys[tok_rows - FILE_MOST :], values[tok_rows - FILE_MOST :]], axis=1),
        "seq",
        1,
    )
    file_count = file_lengths.shape[1]
    batch_pick = (jnp.arange(file_lengths.shape[0], dtype=jnp.int32) == sequence).astype(jnp.int32)
    lengths_here = jnp.sum(file_lengths * batch_pick[:, None], axis=0)
    file_index = jnp.arange(file_count, dtype=jnp.int32)
    upto = (file_index[:, None] <= file_index[None, :]).astype(jnp.int32)
    file_ends = jnp.sum(lengths_here[:, None] * upto, axis=0)
    scale = 1.0 / math.sqrt(HD)
    ordered = attend_ordered(
        owner_of[0].astype(jnp.int32),
        offset.astype(jnp.int32),
        queries,
        keys,
        values,
        rim,
        file_ends,
        scale,
    )
    rows_each = ordered.shape[1] // head_count
    chunks = ordered.reshape(shard_count * head_count, rows_each, ordered.shape[2])
    arrived = lax.all_to_all(chunks, ("seq", "head"), 0, 0, tiled=True)
    arrived = arrived.reshape(shard_count, head_count, rows_each, ordered.shape[2])
    arrived = jnp.transpose(arrived, (0, 2, 1, 3)).reshape(
        shard_count, rows_each, head_count * ordered.shape[2]
    )
    return arrived[None]


def solution(mesh):
    return jax.shard_map(
        per_device,
        mesh=mesh,
        in_specs=(P("seq", "head"), P("seq", "head"), P("seq", "head"), P(), P("seq", None)),
        out_specs=P("seq", None, "head", None),
        check_vma=False,
    )
```

```python
import functools
import math

import jax
import jax.numpy as jnp
from jax import lax
from jax.experimental import pallas as pl
from jax.experimental.pallas import tpu as pltpu
from jax.sharding import PartitionSpec as P

HD = 128
KV_HEADS = 8
FILE_MOST = 512
QROWS = 256
TRIM = 128
TRIMS = 2


def from_behind(block, axis, distance):
    devices = range(lax.axis_size(axis))
    route = [(i - distance, i) for i in devices if i - distance in devices]
    return lax.ppermute(block, axis, route)


def attend_rows(q_ref, k_src, fe_row_ref, fe_col_ref, out_ref, out_start, k_start, first, lo, scale):
    window = QROWS + FILE_MOST - lo
    k_window = k_src[0][pl.ds(pl.multiple_of(k_start + lo, TRIM), window), :]
    v_window = k_src[1][pl.ds(pl.multiple_of(k_start + lo, TRIM), window), :]
    q_pos = first + lax.broadcasted_iota(jnp.int32, (QROWS, 1), 0)
    q_doc = jnp.sum((fe_row_ref[...] <= q_pos).astype(jnp.float32), axis=1, keepdims=True)
    k_pos = first - FILE_MOST + lo + lax.broadcasted_iota(jnp.int32, (1, window), 1)
    k_doc = jnp.sum((fe_col_ref[...] <= k_pos).astype(jnp.float32), axis=0, keepdims=True)
    k_doc = jnp.where(k_pos >= 0, k_doc, -1.0)
    row = lax.broadcasted_iota(jnp.int32, (QROWS, window), 0)
    col = lax.broadcasted_iota(jnp.int32, (QROWS, window), 1)
    allowed = (k_doc == q_doc) & (col + lo <= row + FILE_MOST)
    for g in range(q_ref.shape[1] // HD):
        q_head = q_ref[:, g * HD : (g + 1) * HD]
        scores = (
            lax.dot_general(
                q_head, k_window, (((1,), (1,)), ((), ())), preferred_element_type=jnp.float32
            )
            * scale
        )
        scores = jnp.where(allowed, scores, -jnp.inf)
        row_max = jnp.max(scores, axis=1, keepdims=True)
        expo = jnp.exp(scores - row_max)
        weights = (expo / jnp.sum(expo, axis=1, keepdims=True)).astype(jnp.bfloat16)
        result = jnp.dot(weights, v_window, preferred_element_type=jnp.float32)
        out_ref[pl.ds(out_start, QROWS), g * HD : (g + 1) * HD] = result.astype(out_ref.dtype)


def later_kernel(offset_ref, trim_ref, q_ref, k_ref, v_ref, fe_row_ref, fe_col_ref, o_ref, *, scale, skip):
    step = pl.program_id(0)
    block = step + skip
    k_start = pl.multiple_of(block * QROWS - FILE_MOST, QROWS)
    first = offset_ref[0] + block * QROWS
    for t in range(TRIMS + 1):
        pl.when(trim_ref[block] == t)(
            functools.partial(
                attend_rows, q_ref, (k_ref, v_ref), fe_row_ref, fe_col_ref, o_ref, 0, k_start, first,
                t * TRIM, scale,
            )
        )


def early_kernel(owner_ref, offset_ref, trim_ref, q_ref, k_ref, v_ref, rim_ref, fe_row_ref, fe_col_ref,
                 later_ref, o_ref, wide_k, wide_v, attended, *, scale, piece):
    step = pl.program_id(0)
    lead = wide_k.shape[0] - FILE_MOST

    @pl.when(step == 0)
    def _():
        wide_k[0:FILE_MOST, :] = rim_ref[:, 0:HD]
        wide_k[FILE_MOST:, :] = k_ref[0:lead, :]
        wide_v[0:FILE_MOST, :] = rim_ref[:, HD : 2 * HD]
        wide_v[FILE_MOST:, :] = v_ref[0:lead, :]
        attended[lead:, :] = later_ref[lead:, :]

    start = pl.multiple_of(step * QROWS, QROWS)
    first = offset_ref[0] + step * QROWS
    for t in range(TRIMS + 1):
        pl.when(trim_ref[step] == t)(
            functools.partial(
                attend_rows, q_ref, (wide_k, wide_v), fe_row_ref, fe_col_ref, attended, start, start,
                first, t * TRIM, scale,
            )
        )

    @pl.when(step == pl.num_programs(0) - 1)
    def _():
        for p in range(o_ref.shape[0]):
            o_ref[owner_ref[p]] = attended[p * piece : (p + 1) * piece, :]


def leading_trims(offset, file_ends, block_count):
    firsts = offset + QROWS * jnp.arange(block_count, dtype=jnp.int32)
    starts = jnp.max(jnp.where(file_ends[None, :] <= firsts[:, None], file_ends[None, :], 0), axis=1)
    lasts = firsts[:, None] - FILE_MOST + TRIM - 1 + TRIM * jnp.arange(TRIMS, dtype=jnp.int32)[None, :]
    return jnp.sum((lasts < starts[:, None]).astype(jnp.int32), axis=1)

def attend_ordered(owner_row, offset, queries, keys, values, rim, file_ends, scale):
    tok_rows, width = queries.shape
    shard_count = owner_row.shape[0]
    piece = tok_rows // shard_count
    block_count = tok_rows // QROWS
    early = FILE_MOST // QROWS
    trims = leading_trims(offset, file_ends, block_count)
    offset_row = jnp.reshape(offset, (1,))
    fe_row = file_ends.reshape(1, -1)
    fe_col = file_ends.reshape(-1, 1)
    full = lambda shape: pl.BlockSpec(shape, lambda i, *_: (0,) * len(shape))
    params = pltpu.CompilerParams(dimension_semantics=("arbitrary",))
    later = pl.pallas_call(
        functools.partial(later_kernel, scale=scale, skip=early),
        grid_spec=pltpu.PrefetchScalarGridSpec(
            num_scalar_prefetch=2,
            grid=(block_count - early,),
            in_specs=[
                pl.BlockSpec((QROWS, width), lambda i, *_: (i + early, 0)),
                full(keys.shape), full(values.shape), full(fe_row.shape), full(fe_col.shape),
            ],
            out_specs=pl.BlockSpec((QROWS, width), lambda i, *_: (i + early, 0)),
        ),
        out_shape=jax.ShapeDtypeStruct((tok_rows, width), queries.dtype),
        compiler_params=params,
    )(offset_row, trims, queries, keys, values, fe_row, fe_col)
    return pl.pallas_call(
        functools.partial(early_kernel, scale=scale, piece=piece),
        grid_spec=pltpu.PrefetchScalarGridSpec(
            num_scalar_prefetch=3,
            grid=(early,),
            in_specs=[
                pl.BlockSpec((QROWS, width), lambda i, *_: (i, 0)),
                full(keys.shape), full(values.shape), full(rim.shape),
                full(fe_row.shape), full(fe_col.shape), full(later.shape),
            ],
            out_specs=full((shard_count, piece, width)),
            scratch_shapes=[
                pltpu.VMEM((2 * FILE_MOST, HD), keys.dtype),
                pltpu.VMEM((2 * FILE_MOST, HD), values.dtype),
                pltpu.VMEM((tok_rows, width), queries.dtype),
            ],
        ),
        out_shape=jax.ShapeDtypeStruct((shard_count, piece, width), queries.dtype),
        compiler_params=params,
    )(owner_row, offset_row, trims, queries, keys, values, rim, fe_row, fe_col, later)


def per_device(queries, keys, values, file_lengths, owner_of):
    tok_rows = queries.shape[0]
    heads_here = keys.shape[1] // HD
    shard_count = lax.axis_size("seq")
    head_count = lax.axis_size("head")
    offset = lax.axis_index("seq") * tok_rows
    sequence = lax.axis_index("head") * heads_here // KV_HEADS
    rim = from_behind(
        jnp.concatenate([keys[tok_rows - FILE_MOST :], values[tok_rows - FILE_MOST :]], axis=1),
        "seq",
        1,
    )
    file_count = file_lengths.shape[1]
    batch_pick = (jnp.arange(file_lengths.shape[0], dtype=jnp.int32) == sequence).astype(jnp.int32)
    lengths_here = jnp.sum(file_lengths * batch_pick[:, None], axis=0)
    file_index = jnp.arange(file_count, dtype=jnp.int32)
    upto = (file_index[:, None] <= file_index[None, :]).astype(jnp.int32)
    file_ends = jnp.sum(lengths_here[:, None] * upto, axis=0)
    scale = 1.0 / math.sqrt(HD)
    ordered = attend_ordered(
        owner_of[0].astype(jnp.int32),
        offset.astype(jnp.int32),
        queries,
        keys,
        values,
        rim,
        file_ends,
        scale,
    )
    rows_each = ordered.shape[1] // head_count
    chunks = jnp.transpose(
        ordered.reshape(shard_count, head_count, rows_each, ordered.shape[2]), (1, 0, 2, 3)
    ).reshape(head_count * shard_count, rows_each, ordered.shape[2])
    arrived = lax.all_to_all(chunks, ("head", "seq"), 0, 0, tiled=True)
    arrived = arrived.reshape(head_count, shard_count, rows_each, ordered.shape[2])
    arrived = jnp.transpose(arrived, (1, 2, 0, 3)).reshape(
        shard_count, rows_each, head_count * ordered.shape[2]
    )
    return arrived[None]


def solution(mesh):
    return jax.shard_map(
        per_device,
        mesh=mesh,
        in_specs=(P("seq", "head"), P("seq", "head"), P("seq", "head"), P(), P("seq", None)),
        out_specs=P("seq", None, "head", None),
        check_vma=False,
    )
```

```python
import functools
import math

import jax
import jax.numpy as jnp
from jax import lax
from jax.experimental import pallas as pl
from jax.experimental.pallas import tpu as pltpu
from jax.sharding import PartitionSpec as P

HD = 128
KV_HEADS = 8
FILE_MOST = 512
QROWS = 256
TRIM = 128
TRIMS = 2


def from_behind(block, axis, distance):
    devices = range(lax.axis_size(axis))
    route = [(i - distance, i) for i in devices if i - distance in devices]
    return lax.ppermute(block, axis, route)


def attend_rows(q_ref, k_src, fe_row_ref, fe_col_ref, out_ref, out_start, k_start, first, lo, scale):
    window = QROWS + FILE_MOST - lo
    k_window = k_src[0][pl.ds(pl.multiple_of(k_start + lo, TRIM), window), :]
    v_window = k_src[1][pl.ds(pl.multiple_of(k_start + lo, TRIM), window), :]
    q_pos = first + lax.broadcasted_iota(jnp.int32, (QROWS, 1), 0)
    q_doc = jnp.sum((fe_row_ref[...] <= q_pos).astype(jnp.float32), axis=1, keepdims=True)
    k_pos = first - FILE_MOST + lo + lax.broadcasted_iota(jnp.int32, (1, window), 1)
    k_doc = jnp.sum((fe_col_ref[...] <= k_pos).astype(jnp.float32), axis=0, keepdims=True)
    k_doc = jnp.where(k_pos >= 0, k_doc, -1.0)
    row = lax.broadcasted_iota(jnp.int32, (QROWS, window), 0)
    col = lax.broadcasted_iota(jnp.int32, (QROWS, window), 1)
    allowed = (k_doc == q_doc) & (col + lo <= row + FILE_MOST)
    for g in range(q_ref.shape[1] // HD):
        q_head = q_ref[:, g * HD : (g + 1) * HD]
        scores = (
            lax.dot_general(
                q_head, k_window, (((1,), (1,)), ((), ())), preferred_element_type=jnp.float32
            )
            * scale
        )
        scores = jnp.where(allowed, scores, -jnp.inf)
        row_max = jnp.max(scores, axis=1, keepdims=True)
        expo = jnp.exp(scores - row_max)
        weights = (expo / jnp.sum(expo, axis=1, keepdims=True)).astype(jnp.bfloat16)
        result = jnp.dot(weights, v_window, preferred_element_type=jnp.float32)
        out_ref[pl.ds(out_start, QROWS), g * HD : (g + 1) * HD] = result.astype(out_ref.dtype)


def later_kernel(offset_ref, trim_ref, q_ref, k_ref, v_ref, fe_row_ref, fe_col_ref, o_ref, *, scale, skip):
    step = pl.program_id(0)
    block = step + skip
    k_start = pl.multiple_of(block * QROWS - FILE_MOST, QROWS)
    first = offset_ref[0] + block * QROWS
    for t in range(TRIMS + 1):
        pl.when(trim_ref[block] == t)(
            functools.partial(
                attend_rows, q_ref, (k_ref, v_ref), fe_row_ref, fe_col_ref, o_ref, 0, k_start, first,
                t * TRIM, scale,
            )
        )


def early_kernel(owner_ref, offset_ref, trim_ref, q_ref, k_ref, v_ref, rim_ref, fe_row_ref, fe_col_ref,
                 later_ref, o_ref, wide_k, wide_v, attended, *, scale, piece):
    step = pl.program_id(0)
    lead = attended.shape[0]

    @pl.when(step == 0)
    def _():
        wide_k[0:FILE_MOST, :] = rim_ref[:, 0:HD]
        wide_k[FILE_MOST:, :] = k_ref[0:lead, :]
        wide_v[0:FILE_MOST, :] = rim_ref[:, HD : 2 * HD]
        wide_v[FILE_MOST:, :] = v_ref[0:lead, :]

    start = pl.multiple_of(step * QROWS, QROWS)
    first = offset_ref[0] + step * QROWS
    for t in range(TRIMS + 1):
        pl.when(trim_ref[step] == t)(
            functools.partial(
                attend_rows, q_ref, (wide_k, wide_v), fe_row_ref, fe_col_ref, attended, start, start,
                first, t * TRIM, scale,
            )
        )

    @pl.when(step == pl.num_programs(0) - 1)
    def _():
        for p in range(o_ref.shape[0]):
            top, bottom = p * piece, (p + 1) * piece
            slot = owner_ref[p]
            if bottom <= lead:
                o_ref[slot] = attended[top:bottom, :]
            elif top >= lead:
                o_ref[slot] = later_ref[top:bottom, :]
            else:
                o_ref[slot, 0 : lead - top, :] = attended[top:lead, :]
                o_ref[slot, lead - top : piece, :] = later_ref[lead:bottom, :]


def rim_kernel(k_ref, v_ref, o_ref):
    o_ref[:, 0:HD] = k_ref[...]
    o_ref[:, HD : 2 * HD] = v_ref[...]


def rim_of(keys, values):
    tok_rows = keys.shape[0]
    last = tok_rows // FILE_MOST - 1
    return pl.pallas_call(
        rim_kernel,
        grid=(1,),
        in_specs=[
            pl.BlockSpec((FILE_MOST, HD), lambda i: (last, 0)),
            pl.BlockSpec((FILE_MOST, HD), lambda i: (last, 0)),
        ],
        out_specs=pl.BlockSpec((FILE_MOST, 2 * HD), lambda i: (0, 0)),
        out_shape=jax.ShapeDtypeStruct((FILE_MOST, 2 * HD), keys.dtype),
    )(keys, values)


def leading_trims(offset, file_ends, block_count):
    firsts = offset + QROWS * jnp.arange(block_count, dtype=jnp.int32)
    starts = jnp.max(jnp.where(file_ends[None, :] <= firsts[:, None], file_ends[None, :], 0), axis=1)
    lasts = firsts[:, None] - FILE_MOST + TRIM - 1 + TRIM * jnp.arange(TRIMS, dtype=jnp.int32)[None, :]
    return jnp.sum((lasts < starts[:, None]).astype(jnp.int32), axis=1)

def attend_ordered(owner_row, offset, queries, keys, values, rim, file_ends, scale):
    tok_rows, width = queries.shape
    shard_count = owner_row.shape[0]
    piece = tok_rows // shard_count
    block_count = tok_rows // QROWS
    early = FILE_MOST // QROWS
    trims = leading_trims(offset, file_ends, block_count)
    offset_row = jnp.reshape(offset, (1,))
    fe_row = file_ends.reshape(1, -1)
    fe_col = file_ends.reshape(-1, 1)
    full = lambda shape: pl.BlockSpec(shape, lambda i, *_: (0,) * len(shape))
    params = pltpu.CompilerParams(dimension_semantics=("arbitrary",))
    later = pl.pallas_call(
        functools.partial(later_kernel, scale=scale, skip=early),
        grid_spec=pltpu.PrefetchScalarGridSpec(
            num_scalar_prefetch=2,
            grid=(block_count - early,),
            in_specs=[
                pl.BlockSpec((QROWS, width), lambda i, *_: (i + early, 0)),
                full(keys.shape), full(values.shape), full(fe_row.shape), full(fe_col.shape),
            ],
            out_specs=pl.BlockSpec((QROWS, width), lambda i, *_: (i + early, 0)),
        ),
        out_shape=jax.ShapeDtypeStruct((tok_rows, width), queries.dtype),
        compiler_params=params,
    )(offset_row, trims, queries, keys, values, fe_row, fe_col)
    return pl.pallas_call(
        functools.partial(early_kernel, scale=scale, piece=piece),
        grid_spec=pltpu.PrefetchScalarGridSpec(
            num_scalar_prefetch=3,
            grid=(early,),
            in_specs=[
                pl.BlockSpec((QROWS, width), lambda i, *_: (i, 0)),
                full(keys.shape), full(values.shape), full(rim.shape),
                full(fe_row.shape), full(fe_col.shape), full(later.shape),
            ],
            out_specs=full((shard_count, piece, width)),
            scratch_shapes=[
                pltpu.VMEM((2 * FILE_MOST, HD), keys.dtype),
                pltpu.VMEM((2 * FILE_MOST, HD), values.dtype),
                pltpu.VMEM((FILE_MOST, width), queries.dtype),
            ],
        ),
        out_shape=jax.ShapeDtypeStruct((shard_count, piece, width), queries.dtype),
        compiler_params=params,
    )(owner_row, offset_row, trims, queries, keys, values, rim, fe_row, fe_col, later)


def per_device(queries, keys, values, file_lengths, owner_of):
    tok_rows = queries.shape[0]
    heads_here = keys.shape[1] // HD
    shard_count = lax.axis_size("seq")
    head_count = lax.axis_size("head")
    offset = lax.axis_index("seq") * tok_rows
    sequence = lax.axis_index("head") * heads_here // KV_HEADS
    rim = from_behind(rim_of(keys, values), "seq", 1)
    file_count = file_lengths.shape[1]
    batch_pick = (jnp.arange(file_lengths.shape[0], dtype=jnp.int32) == sequence).astype(jnp.int32)
    lengths_here = jnp.sum(file_lengths * batch_pick[:, None], axis=0)
    file_index = jnp.arange(file_count, dtype=jnp.int32)
    upto = (file_index[:, None] <= file_index[None, :]).astype(jnp.int32)
    file_ends = jnp.sum(lengths_here[:, None] * upto, axis=0)
    scale = 1.0 / math.sqrt(HD)
    ordered = attend_ordered(
        owner_of[0].astype(jnp.int32),
        offset.astype(jnp.int32),
        queries,
        keys,
        values,
        rim,
        file_ends,
        scale,
    )
    rows_each = ordered.shape[1] // head_count
    chunks = ordered.reshape(shard_count * head_count, rows_each, ordered.shape[2])
    arrived = lax.all_to_all(chunks, ("seq", "head"), 0, 0, tiled=True)
    arrived = arrived.reshape(shard_count, head_count, rows_each, ordered.shape[2])
    arrived = jnp.transpose(arrived, (0, 2, 1, 3)).reshape(
        shard_count, rows_each, head_count * ordered.shape[2]
    )
    return arrived[None]


def solution(mesh):
    return jax.shard_map(
        per_device,
        mesh=mesh,
        in_specs=(P("seq", "head"), P("seq", "head"), P("seq", "head"), P(), P("seq", None)),
        out_specs=P("seq", None, "head", None),
        check_vma=False,
    )
```

```python
import functools
import math

import jax
import jax.numpy as jnp
from jax import lax
from jax.experimental import pallas as pl
from jax.experimental.pallas import tpu as pltpu
from jax.sharding import PartitionSpec as P

HD = 128
KV_HEADS = 8
FILE_MOST = 512
QROWS = 256
TRIM = 128
TRIMS = 2


def from_behind(block, axis, distance):
    devices = range(lax.axis_size(axis))
    route = [(i - distance, i) for i in devices if i - distance in devices]
    return lax.ppermute(block, axis, route)


def attend_rows(q_ref, k_src, fe_row_ref, fe_col_ref, out_ref, out_start, k_start, first, lo, scale):
    window = QROWS + FILE_MOST - lo
    k_window = k_src[0][pl.ds(pl.multiple_of(k_start + lo, TRIM), window), :]
    v_window = k_src[1][pl.ds(pl.multiple_of(k_start + lo, TRIM), window), :]
    q_pos = first + lax.broadcasted_iota(jnp.int32, (QROWS, 1), 0)
    q_doc = jnp.sum((fe_row_ref[...] <= q_pos).astype(jnp.float32), axis=1, keepdims=True)
    k_pos = first - FILE_MOST + lo + lax.broadcasted_iota(jnp.int32, (1, window), 1)
    k_doc = jnp.sum((fe_col_ref[...] <= k_pos).astype(jnp.float32), axis=0, keepdims=True)
    k_doc = jnp.where(k_pos >= 0, k_doc, -1.0)
    row = lax.broadcasted_iota(jnp.int32, (QROWS, window), 0)
    col = lax.broadcasted_iota(jnp.int32, (QROWS, window), 1)
    allowed = (k_doc == q_doc) & (col + lo <= row + FILE_MOST)
    for g in range(q_ref.shape[1] // HD):
        q_head = q_ref[:, g * HD : (g + 1) * HD]
        scores = (
            lax.dot_general(
                q_head, k_window, (((1,), (1,)), ((), ())), preferred_element_type=jnp.float32
            )
            * scale
        )
        scores = jnp.where(allowed, scores, -jnp.inf)
        row_max = jnp.max(scores, axis=1, keepdims=True)
        expo = jnp.exp(scores - row_max)
        weights = (expo / jnp.sum(expo, axis=1, keepdims=True)).astype(jnp.bfloat16)
        result = jnp.dot(weights, v_window, preferred_element_type=jnp.float32)
        out_ref[pl.ds(out_start, QROWS), g * HD : (g + 1) * HD] = result.astype(out_ref.dtype)


def later_kernel(owner_ref, offset_ref, trim_ref, q_ref, k_ref, v_ref, fe_row_ref, fe_col_ref, o_ref,
                 attended, *, scale, skip, piece):
    step = pl.program_id(0)
    block = step + skip
    lead = skip * QROWS
    k_start = pl.multiple_of(block * QROWS - FILE_MOST, QROWS)
    first = offset_ref[0] + block * QROWS
    for t in range(TRIMS + 1):
        pl.when(trim_ref[block] == t)(
            functools.partial(
                attend_rows, q_ref, (k_ref, v_ref), fe_row_ref, fe_col_ref, attended,
                pl.multiple_of(step * QROWS, QROWS), k_start, first, t * TRIM, scale,
            )
        )

    @pl.when(step == pl.num_programs(0) - 1)
    def _():
        for p in range(o_ref.shape[0]):
            top, bottom = p * piece, (p + 1) * piece
            if top >= lead:
                o_ref[owner_ref[p]] = attended[top - lead : bottom - lead, :]
            elif bottom > lead:
                o_ref[owner_ref[p], lead - top : piece, :] = attended[0 : bottom - lead, :]


def early_kernel(owner_ref, offset_ref, trim_ref, q_ref, k_ref, v_ref, rim_ref, fe_row_ref, fe_col_ref,
                 later_ref, o_ref, wide_k, wide_v, attended, sems, *, scale, piece):
    del later_ref
    step = pl.program_id(0)
    lead = attended.shape[0]

    @pl.when(step == 0)
    def _():
        wide_k[0:FILE_MOST, :] = rim_ref[:, 0:HD]
        wide_k[FILE_MOST:, :] = k_ref[0:lead, :]
        wide_v[0:FILE_MOST, :] = rim_ref[:, HD : 2 * HD]
        wide_v[FILE_MOST:, :] = v_ref[0:lead, :]

    start = pl.multiple_of(step * QROWS, QROWS)
    first = offset_ref[0] + step * QROWS
    for t in range(TRIMS + 1):
        pl.when(trim_ref[step] == t)(
            functools.partial(
                attend_rows, q_ref, (wide_k, wide_v), fe_row_ref, fe_col_ref, attended, start, start,
                first, t * TRIM, scale,
            )
        )

    @pl.when(step == pl.num_programs(0) - 1)
    def _():
        copies = []
        for p in range(o_ref.shape[0]):
            top, bottom = p * piece, min((p + 1) * piece, lead)
            if top < lead:
                copies.append(
                    pltpu.make_async_copy(
                        attended.at[top:bottom, :],
                        o_ref.at[owner_ref[p], 0 : bottom - top, :],
                        sems.at[p],
                    )
                )
        for copy in copies:
            copy.start()
        for copy in copies:
            copy.wait()


def rim_kernel(k_ref, v_ref, o_ref):
    o_ref[:, 0:HD] = k_ref[...]
    o_ref[:, HD : 2 * HD] = v_ref[...]


def rim_of(keys, values):
    tok_rows = keys.shape[0]
    last = tok_rows // FILE_MOST - 1
    return pl.pallas_call(
        rim_kernel,
        grid=(1,),
        in_specs=[
            pl.BlockSpec((FILE_MOST, HD), lambda i: (last, 0)),
            pl.BlockSpec((FILE_MOST, HD), lambda i: (last, 0)),
        ],
        out_specs=pl.BlockSpec((FILE_MOST, 2 * HD), lambda i: (0, 0)),
        out_shape=jax.ShapeDtypeStruct((FILE_MOST, 2 * HD), keys.dtype),
    )(keys, values)


def leading_trims(offset, file_ends, block_count):
    firsts = offset + QROWS * jnp.arange(block_count, dtype=jnp.int32)
    starts = jnp.max(jnp.where(file_ends[None, :] <= firsts[:, None], file_ends[None, :], 0), axis=1)
    lasts = firsts[:, None] - FILE_MOST + TRIM - 1 + TRIM * jnp.arange(TRIMS, dtype=jnp.int32)[None, :]
    return jnp.sum((lasts < starts[:, None]).astype(jnp.int32), axis=1)

def attend_ordered(owner_row, offset, queries, keys, values, rim, file_ends, scale):
    tok_rows, width = queries.shape
    shard_count = owner_row.shape[0]
    piece = tok_rows // shard_count
    block_count = tok_rows // QROWS
    early = FILE_MOST // QROWS
    trims = leading_trims(offset, file_ends, block_count)
    offset_row = jnp.reshape(offset, (1,))
    fe_row = file_ends.reshape(1, -1)
    fe_col = file_ends.reshape(-1, 1)
    full = lambda shape: pl.BlockSpec(shape, lambda i, *_: (0,) * len(shape))
    params = pltpu.CompilerParams(dimension_semantics=("arbitrary",))
    later = pl.pallas_call(
        functools.partial(later_kernel, scale=scale, skip=early, piece=piece),
        grid_spec=pltpu.PrefetchScalarGridSpec(
            num_scalar_prefetch=3,
            grid=(block_count - early,),
            in_specs=[
                pl.BlockSpec((QROWS, width), lambda i, *_: (i + early, 0)),
                full(keys.shape), full(values.shape), full(fe_row.shape), full(fe_col.shape),
            ],
            out_specs=full((shard_count, piece, width)),
            scratch_shapes=[pltpu.VMEM((tok_rows - early * QROWS, width), queries.dtype)],
        ),
        out_shape=jax.ShapeDtypeStruct((shard_count, piece, width), queries.dtype),
        compiler_params=params,
    )(owner_row, offset_row, trims, queries, keys, values, fe_row, fe_col)
    return pl.pallas_call(
        functools.partial(early_kernel, scale=scale, piece=piece),
        grid_spec=pltpu.PrefetchScalarGridSpec(
            num_scalar_prefetch=3,
            grid=(early,),
            in_specs=[
                pl.BlockSpec((QROWS, width), lambda i, *_: (i, 0)),
                full(keys.shape), full(values.shape), full(rim.shape),
                full(fe_row.shape), full(fe_col.shape), pl.BlockSpec(memory_space=pl.ANY),
            ],
            out_specs=pl.BlockSpec(memory_space=pl.ANY),
            scratch_shapes=[
                pltpu.VMEM((2 * FILE_MOST, HD), keys.dtype),
                pltpu.VMEM((2 * FILE_MOST, HD), values.dtype),
                pltpu.VMEM((early * QROWS, width), queries.dtype),
                pltpu.SemaphoreType.DMA((shard_count,)),
            ],
        ),
        out_shape=jax.ShapeDtypeStruct((shard_count, piece, width), queries.dtype),
        input_output_aliases={9: 0},
        compiler_params=params,
    )(owner_row, offset_row, trims, queries, keys, values, rim, fe_row, fe_col, later)


def per_device(queries, keys, values, file_lengths, owner_of):
    tok_rows = queries.shape[0]
    heads_here = keys.shape[1] // HD
    shard_count = lax.axis_size("seq")
    head_count = lax.axis_size("head")
    offset = lax.axis_index("seq") * tok_rows
    sequence = lax.axis_index("head") * heads_here // KV_HEADS
    rim = from_behind(rim_of(keys, values), "seq", 1)
    file_count = file_lengths.shape[1]
    batch_pick = (jnp.arange(file_lengths.shape[0], dtype=jnp.int32) == sequence).astype(jnp.int32)
    lengths_here = jnp.sum(file_lengths * batch_pick[:, None], axis=0)
    file_index = jnp.arange(file_count, dtype=jnp.int32)
    upto = (file_index[:, None] <= file_index[None, :]).astype(jnp.int32)
    file_ends = jnp.sum(lengths_here[:, None] * upto, axis=0)
    scale = 1.0 / math.sqrt(HD)
    ordered = attend_ordered(
        owner_of[0].astype(jnp.int32),
        offset.astype(jnp.int32),
        queries,
        keys,
        values,
        rim,
        file_ends,
        scale,
    )
    rows_each = ordered.shape[1] // head_count
    chunks = ordered.reshape(shard_count * head_count, rows_each, ordered.shape[2])
    arrived = lax.all_to_all(chunks, ("seq", "head"), 0, 0, tiled=True)
    arrived = arrived.reshape(shard_count, head_count, rows_each, ordered.shape[2])
    arrived = jnp.transpose(arrived, (0, 2, 1, 3)).reshape(
        shard_count, rows_each, head_count * ordered.shape[2]
    )
    return arrived[None]


def solution(mesh):
    return jax.shard_map(
        per_device,
        mesh=mesh,
        in_specs=(P("seq", "head"), P("seq", "head"), P("seq", "head"), P(), P("seq", None)),
        out_specs=P("seq", None, "head", None),
        check_vma=False,
    )
```

```python
import functools
import math

import jax
import jax.numpy as jnp
from jax import lax
from jax.experimental import pallas as pl
from jax.experimental.pallas import tpu as pltpu
from jax.sharding import PartitionSpec as P

HD = 128
KV_HEADS = 8
FILE_MOST = 512
QROWS = 256
TRIM = 128
TRIMS = 2


def from_behind(block, axis, distance):
    devices = range(lax.axis_size(axis))
    route = [(i - distance, i) for i in devices if i - distance in devices]
    return lax.ppermute(block, axis, route)


def attend_rows(q_ref, k_src, fe_row_ref, fe_col_ref, out_ref, out_start, k_start, first, lo, scale):
    window = QROWS + FILE_MOST - lo
    k_window = k_src[0][pl.ds(pl.multiple_of(k_start + lo, TRIM), window), :]
    v_window = k_src[1][pl.ds(pl.multiple_of(k_start + lo, TRIM), window), :]
    q_pos = first + lax.broadcasted_iota(jnp.int32, (QROWS, 1), 0)
    q_doc = jnp.sum((fe_row_ref[...] <= q_pos).astype(jnp.float32), axis=1, keepdims=True)
    k_pos = first - FILE_MOST + lo + lax.broadcasted_iota(jnp.int32, (1, window), 1)
    k_pos_col = first - FILE_MOST + lo + lax.broadcasted_iota(jnp.int32, (window, 1), 0)
    ended = (fe_row_ref[...] <= k_pos_col).astype(jnp.bfloat16)
    ones = jnp.ones((8, ended.shape[1]), jnp.bfloat16)
    k_doc = lax.dot_general(
        ones, ended, (((1,), (1,)), ((), ())), preferred_element_type=jnp.float32
    )[0:1]
    k_doc = jnp.where(k_pos >= 0, k_doc, -1.0)
    row = lax.broadcasted_iota(jnp.int32, (QROWS, window), 0)
    col = lax.broadcasted_iota(jnp.int32, (QROWS, window), 1)
    allowed = (k_doc == q_doc) & (col + lo <= row + FILE_MOST)
    for g in range(q_ref.shape[1] // HD):
        q_head = q_ref[:, g * HD : (g + 1) * HD]
        scores = (
            lax.dot_general(
                q_head, k_window, (((1,), (1,)), ((), ())), preferred_element_type=jnp.float32
            )
            * scale
        )
        scores = jnp.where(allowed, scores, -jnp.inf)
        row_max = jnp.max(scores, axis=1, keepdims=True)
        expo = jnp.exp(scores - row_max)
        weights = (expo / jnp.sum(expo, axis=1, keepdims=True)).astype(jnp.bfloat16)
        result = jnp.dot(weights, v_window, preferred_element_type=jnp.float32)
        out_ref[pl.ds(out_start, QROWS), g * HD : (g + 1) * HD] = result.astype(out_ref.dtype)


def later_kernel(owner_ref, offset_ref, trim_ref, q_ref, k_ref, v_ref, fe_row_ref, fe_col_ref, o_ref,
                 attended, *, scale, skip, piece):
    step = pl.program_id(0)
    block = step + skip
    lead = skip * QROWS
    k_start = pl.multiple_of(block * QROWS - FILE_MOST, QROWS)
    first = offset_ref[0] + block * QROWS
    for t in range(TRIMS + 1):
        pl.when(trim_ref[block] == t)(
            functools.partial(
                attend_rows, q_ref, (k_ref, v_ref), fe_row_ref, fe_col_ref, attended,
                pl.multiple_of(step * QROWS, QROWS), k_start, first, t * TRIM, scale,
            )
        )

    @pl.when(step == pl.num_programs(0) - 1)
    def _():
        for p in range(o_ref.shape[0]):
            top, bottom = p * piece, (p + 1) * piece
            if top >= lead:
                o_ref[owner_ref[p]] = attended[top - lead : bottom - lead, :]
            elif bottom > lead:
                o_ref[owner_ref[p], lead - top : piece, :] = attended[0 : bottom - lead, :]


def early_kernel(owner_ref, offset_ref, trim_ref, q_ref, k_ref, v_ref, rim_ref, fe_row_ref, fe_col_ref,
                 later_ref, o_ref, wide_k, wide_v, attended, sems, *, scale, piece):
    del later_ref
    step = pl.program_id(0)
    lead = attended.shape[0]

    @pl.when(step == 0)
    def _():
        wide_k[0:FILE_MOST, :] = rim_ref[:, 0:HD]
        wide_k[FILE_MOST:, :] = k_ref[0:lead, :]
        wide_v[0:FILE_MOST, :] = rim_ref[:, HD : 2 * HD]
        wide_v[FILE_MOST:, :] = v_ref[0:lead, :]

    start = pl.multiple_of(step * QROWS, QROWS)
    first = offset_ref[0] + step * QROWS
    for t in range(TRIMS + 1):
        pl.when(trim_ref[step] == t)(
            functools.partial(
                attend_rows, q_ref, (wide_k, wide_v), fe_row_ref, fe_col_ref, attended, start, start,
                first, t * TRIM, scale,
            )
        )

    @pl.when(step == pl.num_programs(0) - 1)
    def _():
        copies = []
        for p in range(o_ref.shape[0]):
            top, bottom = p * piece, min((p + 1) * piece, lead)
            if top < lead:
                copies.append(
                    pltpu.make_async_copy(
                        attended.at[top:bottom, :],
                        o_ref.at[owner_ref[p], 0 : bottom - top, :],
                        sems.at[p],
                    )
                )
        for copy in copies:
            copy.start()
        for copy in copies:
            copy.wait()


def rim_kernel(k_ref, v_ref, o_ref):
    o_ref[:, 0:HD] = k_ref[...]
    o_ref[:, HD : 2 * HD] = v_ref[...]


def rim_of(keys, values):
    tok_rows = keys.shape[0]
    last = tok_rows // FILE_MOST - 1
    return pl.pallas_call(
        rim_kernel,
        grid=(1,),
        in_specs=[
            pl.BlockSpec((FILE_MOST, HD), lambda i: (last, 0)),
            pl.BlockSpec((FILE_MOST, HD), lambda i: (last, 0)),
        ],
        out_specs=pl.BlockSpec((FILE_MOST, 2 * HD), lambda i: (0, 0)),
        out_shape=jax.ShapeDtypeStruct((FILE_MOST, 2 * HD), keys.dtype),
    )(keys, values)


def leading_trims(offset, file_ends, block_count):
    firsts = offset + QROWS * jnp.arange(block_count, dtype=jnp.int32)
    starts = jnp.max(jnp.where(file_ends[None, :] <= firsts[:, None], file_ends[None, :], 0), axis=1)
    lasts = firsts[:, None] - FILE_MOST + TRIM - 1 + TRIM * jnp.arange(TRIMS, dtype=jnp.int32)[None, :]
    return jnp.sum((lasts < starts[:, None]).astype(jnp.int32), axis=1)

def attend_ordered(owner_row, offset, queries, keys, values, rim, file_ends, scale):
    tok_rows, width = queries.shape
    shard_count = owner_row.shape[0]
    piece = tok_rows // shard_count
    block_count = tok_rows // QROWS
    early = FILE_MOST // QROWS
    trims = leading_trims(offset, file_ends, block_count)
    offset_row = jnp.reshape(offset, (1,))
    fe_row = file_ends.reshape(1, -1)
    fe_col = file_ends.reshape(-1, 1)
    full = lambda shape: pl.BlockSpec(shape, lambda i, *_: (0,) * len(shape))
    params = pltpu.CompilerParams(dimension_semantics=("arbitrary",))
    later = pl.pallas_call(
        functools.partial(later_kernel, scale=scale, skip=early, piece=piece),
        grid_spec=pltpu.PrefetchScalarGridSpec(
            num_scalar_prefetch=3,
            grid=(block_count - early,),
            in_specs=[
                pl.BlockSpec((QROWS, width), lambda i, *_: (i + early, 0)),
                full(keys.shape), full(values.shape), full(fe_row.shape), full(fe_col.shape),
            ],
            out_specs=full((shard_count, piece, width)),
            scratch_shapes=[pltpu.VMEM((tok_rows - early * QROWS, width), queries.dtype)],
        ),
        out_shape=jax.ShapeDtypeStruct((shard_count, piece, width), queries.dtype),
        compiler_params=params,
    )(owner_row, offset_row, trims, queries, keys, values, fe_row, fe_col)
    return pl.pallas_call(
        functools.partial(early_kernel, scale=scale, piece=piece),
        grid_spec=pltpu.PrefetchScalarGridSpec(
            num_scalar_prefetch=3,
            grid=(early,),
            in_specs=[
                pl.BlockSpec((QROWS, width), lambda i, *_: (i, 0)),
                full(keys.shape), full(values.shape), full(rim.shape),
                full(fe_row.shape), full(fe_col.shape), pl.BlockSpec(memory_space=pl.ANY),
            ],
            out_specs=pl.BlockSpec(memory_space=pl.ANY),
            scratch_shapes=[
                pltpu.VMEM((2 * FILE_MOST, HD), keys.dtype),
                pltpu.VMEM((2 * FILE_MOST, HD), values.dtype),
                pltpu.VMEM((early * QROWS, width), queries.dtype),
                pltpu.SemaphoreType.DMA((shard_count,)),
            ],
        ),
        out_shape=jax.ShapeDtypeStruct((shard_count, piece, width), queries.dtype),
        input_output_aliases={9: 0},
        compiler_params=params,
    )(owner_row, offset_row, trims, queries, keys, values, rim, fe_row, fe_col, later)


def per_device(queries, keys, values, file_lengths, owner_of):
    tok_rows = queries.shape[0]
    heads_here = keys.shape[1] // HD
    shard_count = lax.axis_size("seq")
    head_count = lax.axis_size("head")
    offset = lax.axis_index("seq") * tok_rows
    sequence = lax.axis_index("head") * heads_here // KV_HEADS
    rim = from_behind(rim_of(keys, values), "seq", 1)
    file_count = file_lengths.shape[1]
    batch_pick = (jnp.arange(file_lengths.shape[0], dtype=jnp.int32) == sequence).astype(jnp.int32)
    lengths_here = jnp.sum(file_lengths * batch_pick[:, None], axis=0)
    file_index = jnp.arange(file_count, dtype=jnp.int32)
    upto = (file_index[:, None] <= file_index[None, :]).astype(jnp.int32)
    file_ends = jnp.sum(lengths_here[:, None] * upto, axis=0)
    scale = 1.0 / math.sqrt(HD)
    ordered = attend_ordered(
        owner_of[0].astype(jnp.int32),
        offset.astype(jnp.int32),
        queries,
        keys,
        values,
        rim,
        file_ends,
        scale,
    )
    rows_each = ordered.shape[1] // head_count
    chunks = ordered.reshape(shard_count * head_count, rows_each, ordered.shape[2])
    arrived = lax.all_to_all(chunks, ("seq", "head"), 0, 0, tiled=True)
    arrived = arrived.reshape(shard_count, head_count, rows_each, ordered.shape[2])
    arrived = jnp.transpose(arrived, (0, 2, 1, 3)).reshape(
        shard_count, rows_each, head_count * ordered.shape[2]
    )
    return arrived[None]


def solution(mesh):
    return jax.shard_map(
        per_device,
        mesh=mesh,
        in_specs=(P("seq", "head"), P("seq", "head"), P("seq", "head"), P(), P("seq", None)),
        out_specs=P("seq", None, "head", None),
        check_vma=False,
    )
```
